1024 devices in a mesh: pipe: 8 (over y), ctx: 32 (over x, z_lo, core), tp: 4 (over z_hi).
Axes of the slice: x: 4, y: 8, z: 16 (z_hi: 4, z_lo: 4; z = z_hi * 4 + z_lo), core: 2. Of those that a mesh axis runs over, the one named last changes fastest.
Arguments:
- sent: bfloat16 [8, 4096, 5376], P('pipe', 'ctx', 'tp'), may hold values from -6 to 6
- queries: bfloat16 [8, 4096, 2048], P('pipe', 'ctx', 'tp'), may hold values from -6 to 6
- keys: bfloat16 [8, 4096, 1024], P('pipe', 'ctx', 'tp'), may hold values from -6 to 6
- values: bfloat16 [8, 4096, 1024], P('pipe', 'ctx', 'tp'), may hold values from -6 to 6
- segments: int32 [8, 4096], P('pipe', 'ctx'), may hold values from 0 to 3, never falling along the last dimension, each value on 1 to 2048 neighbouring positions
- out_weight: bfloat16 [8, 2048, 5376], P('pipe', 'tp'), may hold values from -0.08396893 to 0.08396893
- norm_gain: float32 [8, 5376], P('pipe', 'tp'), may hold values from 0.5 to 1.5
Outputs:
- emitted: bfloat16 [8, 4096, 5376], P('pipe', 'ctx', 'tp')
The draws below stay inside these ranges and needn't reach their ends.
Inputs may be any that keep to these rules, and one draw needn't show every extreme that they name: `segments`: segment numbers never fall along a micro-batch; every one of the 4 documents has a token.
All inputs are finite; a program needn't handle non-finite values.
Results may differ from the reference program's by a relative error of at most 0.012.
Values may be sent and summed in bfloat16 or wider, within the bound.
No kernel may reach another device: no remote copies, remote signals or barrier semaphores. Data moves between devices by JAX's collectives and lax.ppermute only.
A program may use at most 32 MiB of HBM per device.

```python
import math
import jax
import jax.numpy as jnp
import numpy as np
from jax import lax

D = 5376
HQ = 16
HK = 8
HEAD = 128
SEGS = 4
TOKENS = 4096
SECTIONS = 8
N_TP = 4


def draw_queries(key, part):
    base = jax.random.truncated_normal(jax.random.fold_in(key, 1), -6.0, 6.0, (SECTIONS, TOKENS, HQ * HEAD), jnp.float32)
    return base.astype(jnp.bfloat16)


def draw_keys(key, part):
    base = jax.random.truncated_normal(jax.random.fold_in(key, 2), -6.0, 6.0, (SECTIONS, TOKENS, HK * HEAD), jnp.float32)
    return base.astype(jnp.bfloat16)


def draw_out_weight(key, part):
    base = jax.random.normal(jax.random.fold_in(key, 3), (SECTIONS, HQ * HEAD, D), jnp.float32)
    base = jnp.clip(base, -2.5, 2.5) * (HQ * HEAD) ** (-0.5)
    ramp = 0.5 + jnp.arange(D, dtype=jnp.float32) / (D - 1)
    amplitude = 2.0 - ramp
    return (base * amplitude[None, None, :]).astype(jnp.bfloat16)


def shard_levels(rng, extent, cuts, smallest, high):
    def one(position, shards_of):
        heights = jax.random.uniform(jax.random.fold_in(jax.random.fold_in(rng, 6), position), (shards_of,), jnp.float32, smallest / len(cuts), high / len(cuts))
        return jnp.repeat(jnp.exp(heights), extent[position] // shards_of).reshape((-1,) + (1,) * (len(extent) - position - 1))

    loudness = one(*cuts[0])
    for cut in cuts[1:]:
        loudness = loudness * one(*cut)
    return loudness


def length_profile(number_of, total, limit, lean):
    weights = [(1 << 20) // math.isqrt(rank ** lean) + 1 for rank in range(2, number_of + 1)]
    rest, counts = total - limit - (number_of - 1), [1] * (number_of - 1)
    while rest > 0:
        movable = [i for i in range(number_of - 1) if counts[i] < limit]
        pool, budget = sum([weights[i] for i in movable]), rest
        for i in movable:
            addition = min(limit - counts[i], max(1, budget * weights[i] // pool), rest)
            counts[i] = counts[i] + addition
            rest = rest - addition
    return np.array([limit] + counts)


def ragged(key, amount, total, bound, skew):
    if amount == 2:
        one = jax.random.randint(key, (), max(1, total - bound), min(bound, total - 1) + 1)
        return jnp.stack([one, total - one])
    tallies = jnp.asarray(length_profile(amount, total, bound, skew), jnp.int32)
    couples = (amount - 1) // 2
    donor, receiver = tallies[1:1 + 2 * couples:2], tallies[2:2 + 2 * couples:2]
    room = jnp.minimum(donor - 1, bound - receiver)
    shifted = jax.random.randint(jax.random.fold_in(key, 1), (couples,), 0, 1 << 20) % (room + 1)
    tallies = tallies.at[1:1 + 2 * couples:2].set(donor - shifted).at[2:2 + 2 * couples:2].set(receiver + shifted)
    return tallies[jax.random.permutation(jax.random.fold_in(key, 2), amount)]


def scatter_about(rng, extent, width, most, split=(), kind=jnp.bfloat16):
    array = width * jax.random.normal(rng, extent, jnp.float32)
    if split:
        array = array * shard_levels(rng, extent, split, -0.22, 0.18)
    return jnp.clip(array, -most, most).astype(kind)


def setup_inputs(seed: int = 0) -> dict:
    key_of = jax.random.split(jax.random.key(seed), 8)
    sent = scatter_about(key_of[0], (SECTIONS, TOKENS, D), 1.0, 6.0, ((0, 8), (1, 32), (2, 4)))
    queries = draw_queries(jax.random.fold_in(key_of[7], 71), 0)
    keys = draw_keys(jax.random.fold_in(key_of[7], 71), 0)
    values = scatter_about(key_of[3], (SECTIONS, TOKENS, HK * HEAD), 1.0, 6.0, ((0, 8), (1, 32), (2, 4)))
    segments = jax.vmap(lambda own: jnp.searchsorted(jnp.cumsum(ragged(own, SEGS, TOKENS, TOKENS // 2, 0)), jnp.arange(TOKENS), side="right"))(jax.random.split(key_of[4], SECTIONS)).reshape((SECTIONS, TOKENS)).astype(jnp.int32)
    out_weight = draw_out_weight(jax.random.fold_in(key_of[7], 71), 0)
    norm_gain = jnp.clip(1.0 + 0.1 * jax.random.normal(key_of[6], (SECTIONS, D), jnp.float32), 0.5, 1.5)
    return dict(sent=sent, queries=queries, keys=keys, values=values, segments=segments, out_weight=out_weight, norm_gain=norm_gain)


def section_attention(queries_section, keys_section, values_section, segment_section):
    group_size = HQ // HK
    query_heads = queries_section.reshape(TOKENS, HQ, HEAD).transpose(1, 0, 2)
    key_heads = jnp.repeat(keys_section.reshape(TOKENS, HK, HEAD).transpose(1, 0, 2), group_size, axis=0)
    value_heads = jnp.repeat(values_section.reshape(TOKENS, HK, HEAD).transpose(1, 0, 2), group_size, axis=0)
    positions = jnp.arange(TOKENS, dtype=jnp.int32)
    allowed = (positions[None, :] <= positions[:, None]) & (segment_section[None, :] == segment_section[:, None])
    scale = HEAD ** (-0.5)

    def one_head(operands):
        query_one, key_one, value_one = operands
        scores = jnp.dot(query_one, key_one.T, preferred_element_type=jnp.float32) * scale
        masked = jnp.where(allowed, scores, -1e+30)
        top_score = lax.optimization_barrier(jnp.max(masked, axis=-1, keepdims=True))
        weights = jnp.where(allowed, jnp.exp(masked - top_score), 0.0)
        denom = lax.optimization_barrier(jnp.sum(weights, axis=-1, keepdims=True))
        mixed = jnp.dot(weights.astype(jnp.bfloat16), value_one, preferred_element_type=jnp.float32)
        return mixed / denom
    outputs = lax.map(one_head, (query_heads, key_heads, value_heads))
    return outputs.transpose(1, 0, 2).reshape(TOKENS, HQ * HEAD).astype(jnp.bfloat16)

def reference(sent, queries, keys, values, segments, out_weight, norm_gain):
    incoming = jnp.concatenate([sent[:1], sent[:-1]], axis=0)
    group_rows = HQ * HEAD // N_TP

    def one_section(operands):
        incoming_section, queries_section, keys_section, values_section, segment_section, weight_section, gain_section = operands
        attn = section_attention(queries_section, keys_section, values_section, segment_section)
        branch = jnp.zeros((TOKENS, D), jnp.float32)
        for group_index in range(N_TP):
            lower = group_index * group_rows
            product = jnp.dot(attn[:, lower:lower + group_rows], weight_section[lower:lower + group_rows], preferred_element_type=jnp.float32)
            rounded = lax.optimization_barrier(product.astype(jnp.bfloat16))
            branch = branch + rounded.astype(jnp.float32)
        mean_square = lax.optimization_barrier(jnp.mean(branch * branch, axis=-1, keepdims=True))
        normed = branch * lax.rsqrt(mean_square + 1e-06) * gain_section[None, :]
        return (incoming_section.astype(jnp.float32) + normed).astype(jnp.bfloat16)
    return lax.map(one_section, (incoming, queries, keys, values, segments, out_weight, norm_gain))
```

```python
import jax
import jax.numpy as jnp
from jax import lax
from jax.sharding import PartitionSpec as P

D = 5376
HEAD = 128
LONGEST_DOC = 2048


def shifted(block, axis, distance, size):
    route = [(i, i + distance) for i in range(size) if i + distance < size]
    return lax.ppermute(block, axis, route)


def rotated(block, axis, distance, size):
    route = [(i, (i + distance) % size) for i in range(size)]
    return lax.ppermute(block, axis, route)


def body(sent, queries, keys, values, segments, out_weight, norm_gain):
    n_pipe = lax.axis_size("pipe")
    n_ctx = lax.axis_size("ctx")
    n_tp = lax.axis_size("tp")

    with jax.named_scope("relay"):
        arrived_stream = shifted(sent, "pipe", 1, n_pipe)[0]
        section_index = lax.axis_index("pipe")
        incoming = jnp.where(section_index == 0, sent[0], arrived_stream)

    query_local = queries[0]
    tok_rows = query_local.shape[0]
    kv_heads = keys.shape[2] // HEAD
    query_heads = query_local.shape[1] // HEAD
    group_size = query_heads // kv_heads
    kv_width = kv_heads * HEAD
    scale = HEAD ** (-0.5)
    ctx_index = lax.axis_index("ctx")
    first_pos = ctx_index * tok_rows

    back = min(n_ctx - 1, -(-(LONGEST_DOC - 1) // tok_rows))

    with jax.named_scope("kv_exchange"):
        own_docs = segments[0]
        doc_row = jnp.zeros((16, 2 * kv_width), jnp.bfloat16)
        doc_row = doc_row.at[0, :tok_rows].set(own_docs.astype(jnp.bfloat16))
        packed = jnp.concatenate(
            [jnp.concatenate([keys[0], values[0]], axis=1), doc_row], axis=0
        )
        blocks = [shifted(packed, "ctx", d, n_ctx) for d in range(back, 0, -1)]
        blocks.append(packed)
        stacked = jnp.stack(blocks)

    with jax.named_scope("attention"):
        n_keys = (back + 1) * tok_rows
        key_rows = stacked[:, :tok_rows, :kv_width].reshape(n_keys, kv_heads, HEAD)
        value_rows = stacked[:, :tok_rows, kv_width:].reshape(n_keys, kv_heads, HEAD)
        key_docs = stacked[:, tok_rows, :tok_rows].reshape(n_keys).astype(jnp.int32)
        key_pos = (ctx_index - back) * tok_rows + jnp.arange(n_keys, dtype=jnp.int32)
        query_pos = first_pos + jnp.arange(tok_rows, dtype=jnp.int32)
        allowed = (
            (key_pos[None, :] <= query_pos[:, None])
            & (key_pos[None, :] >= 0)
            & (key_docs[None, :] == own_docs[:, None])
        )
        query_split = query_local.reshape(tok_rows, kv_heads, group_size, HEAD)
        scores = (
            jnp.einsum("tkgd,nkd->kgtn", query_split, key_rows, preferred_element_type=jnp.float32)
            * scale
        )
        masked = jnp.where(allowed, scores, -1e30)
        top = jnp.max(masked, axis=-1, keepdims=True)
        weights = jnp.where(allowed, jnp.exp(masked - top), 0.0)
        denom = jnp.sum(weights, axis=-1)
        mixed = jnp.einsum(
            "kgtn,nkd->tkgd",
            weights.astype(jnp.bfloat16),
            value_rows,
            preferred_element_type=jnp.float32,
        )
        attention = (mixed / denom.transpose(2, 0, 1)[..., None]).reshape(
            tok_rows, query_heads * HEAD
        ).astype(jnp.bfloat16)

    with jax.named_scope("projection"):
        projected = jnp.dot(attention, out_weight[0], preferred_element_type=jnp.float32)
        branch = lax.psum_scatter(
            projected.astype(jnp.bfloat16), "tp", scatter_dimension=1, tiled=True
        ).astype(jnp.float32)

    with jax.named_scope("norm"):
        square_sum = jnp.sum(branch * branch, axis=-1)
        total = square_sum
        for d in range(1, n_tp):
            total = total + rotated(square_sum, "tp", d, n_tp)
        mean_square = total / D
        normed = branch * lax.rsqrt(mean_square + 1e-06)[:, None] * norm_gain[0][None, :]
        emitted = (incoming.astype(jnp.float32) + normed).astype(jnp.bfloat16)
    return emitted[None]


def solution(mesh):
    return jax.shard_map(
        body,
        mesh=mesh,
        in_specs=(
            P("pipe", "ctx", "tp"),
            P("pipe", "ctx", "tp"),
            P("pipe", "ctx", "tp"),
            P("pipe", "ctx", "tp"),
            P("pipe", "ctx"),
            P("pipe", "tp", None),
            P("pipe", "tp"),
        ),
        out_specs=P("pipe", "ctx", "tp"),
        check_vma=False,
    )
```

```python
import jax
import jax.numpy as jnp
from jax import lax
from jax.sharding import PartitionSpec as P

D = 5376
HEAD = 128
LONGEST_DOC = 2048


def shifted(block, axis, distance, size):
    route = [(i, i + distance) for i in range(size) if i + distance < size]
    return lax.ppermute(block, axis, route)


def rotated(block, axis, distance, size):
    route = [(i, (i + distance) % size) for i in range(size)]
    return lax.ppermute(block, axis, route)


def ring_reduce_scatter(product, size):
    rows, width = product.shape
    cols = width // size
    half = rows // 2
    me = lax.axis_index("tp")

    def chunk(part, index):
        start = (lax.rem(index + 2 * size, size)) * cols
        return lax.dynamic_slice_in_dim(part, start, cols, axis=1)

    upper, lower = product[:half], product[half:]
    forward = chunk(upper, me - 1)
    backward = chunk(lower, me + 1)
    for step in range(1, size):
        forward = rotated(forward, "tp", 1, size)
        backward = rotated(backward, "tp", size - 1, size)
        forward = forward.astype(jnp.float32) + chunk(upper, me - 1 - step).astype(jnp.float32)
        backward = backward.astype(jnp.float32) + chunk(lower, me + 1 + step).astype(jnp.float32)
        if step < size - 1:
            forward = forward.astype(jnp.bfloat16)
            backward = backward.astype(jnp.bfloat16)
    return jnp.concatenate([forward, backward], axis=0)


def body(sent, queries, keys, values, segments, out_weight, norm_gain):
    n_pipe = lax.axis_size("pipe")
    n_ctx = lax.axis_size("ctx")
    n_tp = lax.axis_size("tp")

    with jax.named_scope("relay"):
        arrived_stream = shifted(sent, "pipe", 1, n_pipe)[0]
        section_index = lax.axis_index("pipe")
        incoming = jnp.where(section_index == 0, sent[0], arrived_stream)

    query_local = queries[0]
    tok_rows = query_local.shape[0]
    kv_heads = keys.shape[2] // HEAD
    query_heads = query_local.shape[1] // HEAD
    group_size = query_heads // kv_heads
    kv_width = kv_heads * HEAD
    scale = HEAD ** (-0.5)
    ctx_index = lax.axis_index("ctx")
    first_pos = ctx_index * tok_rows

    back = min(n_ctx - 1, -(-(LONGEST_DOC - 1) // tok_rows))

    with jax.named_scope("kv_exchange"):
        own_docs = segments[0]
        doc_row = jnp.zeros((16, 2 * kv_width), jnp.bfloat16)
        doc_row = doc_row.at[0, :tok_rows].set(own_docs.astype(jnp.bfloat16))
        packed = jnp.concatenate(
            [jnp.concatenate([keys[0], values[0]], axis=1), doc_row], axis=0
        )
        near = [shifted(packed, "ctx", d, n_ctx) for d in (3, 2, 1)]
        oldest = shifted(packed, "ctx", back, n_ctx) if back > 3 else None
        quad = jnp.stack(near + [packed])
        blocks = [quad]
        reach = 4
        while reach + 3 < back:
            blocks.insert(0, shifted(quad, "ctx", reach, n_ctx))
            reach += 4
        if oldest is not None:
            blocks.insert(0, oldest[None])
        stacked = jnp.concatenate(blocks, axis=0)
        assert stacked.shape[0] == back + 1

    with jax.named_scope("attention"):
        n_keys = (back + 1) * tok_rows
        key_rows = stacked[:, :tok_rows, :kv_width].reshape(n_keys, kv_heads, HEAD)
        value_rows = stacked[:, :tok_rows, kv_width:].reshape(n_keys, kv_heads, HEAD)
        key_docs = stacked[:, tok_rows, :tok_rows].reshape(n_keys).astype(jnp.int32)
        key_pos = (ctx_index - back) * tok_rows + jnp.arange(n_keys, dtype=jnp.int32)
        query_pos = first_pos + jnp.arange(tok_rows, dtype=jnp.int32)
        allowed = (
            (key_pos[None, :] <= query_pos[:, None])
            & (key_pos[None, :] >= 0)
            & (key_docs[None, :] == own_docs[:, None])
        )
        query_split = query_local.reshape(tok_rows, kv_heads, group_size, HEAD)
        scores = (
            jnp.einsum("tkgd,nkd->kgtn", query_split, key_rows, preferred_element_type=jnp.float32)
            * scale
        )
        masked = jnp.where(allowed, scores, -1e30)
        top = jnp.max(masked, axis=-1, keepdims=True)
        weights = jnp.where(allowed, jnp.exp(masked - top), 0.0)
        denom = jnp.sum(weights, axis=-1)
        mixed = jnp.einsum(
            "kgtn,nkd->tkgd",
            weights.astype(jnp.bfloat16),
            value_rows,
            preferred_element_type=jnp.float32,
        )
        attention = (mixed / denom.transpose(2, 0, 1)[..., None]).reshape(
            tok_rows, query_heads * HEAD
        ).astype(jnp.bfloat16)

    with jax.named_scope("projection"):
        projected = jnp.dot(attention, out_weight[0], preferred_element_type=jnp.float32)
        branch = ring_reduce_scatter(projected.astype(jnp.bfloat16), n_tp)

    with jax.named_scope("norm"):
        square_sum = jnp.sum(branch * branch, axis=-1)
        total = square_sum
        for d in range(1, n_tp):
            total = total + rotated(square_sum, "tp", d, n_tp)
        mean_square = total / D
        normed = branch * lax.rsqrt(mean_square + 1e-06)[:, None] * norm_gain[0][None, :]
        emitted = (incoming.astype(jnp.float32) + normed).astype(jnp.bfloat16)
    return emitted[None]


def solution(mesh):
    return jax.shard_map(
        body,
        mesh=mesh,
        in_specs=(
            P("pipe", "ctx", "tp"),
            P("pipe", "ctx", "tp"),
            P("pipe", "ctx", "tp"),
            P("pipe", "ctx", "tp"),
            P("pipe", "ctx"),
            P("pipe", "tp", None),
            P("pipe", "tp"),
        ),
        out_specs=P("pipe", "ctx", "tp"),
        check_vma=False,
    )
```

```python
import jax
import jax.numpy as jnp
from jax import lax
from jax.sharding import PartitionSpec as P

D = 5376
HEAD = 128
LONGEST_DOC = 2048


def shifted(block, axis, distance, size):
    route = [(i, i + distance) for i in range(size) if i + distance < size]
    return lax.ppermute(block, axis, route)


def rotated(block, axis, distance, size):
    route = [(i, (i + distance) % size) for i in range(size)]
    return lax.ppermute(block, axis, route)


def ring_reduce_scatter(product, size):
    rows, width = product.shape
    cols = width // size
    half = rows // 2
    me = lax.axis_index("tp")

    def chunk(part, index):
        start = (lax.rem(index + 2 * size, size)) * cols
        return lax.dynamic_slice_in_dim(part, start, cols, axis=1)

    upper, lower = product[:half], product[half:]
    forward = chunk(upper, me - 1)
    backward = chunk(lower, me + 1)
    for step in range(1, size):
        forward = rotated(forward, "tp", 1, size)
        backward = rotated(backward, "tp", size - 1, size)
        forward = forward.astype(jnp.float32) + chunk(upper, me - 1 - step).astype(jnp.float32)
        backward = backward.astype(jnp.float32) + chunk(lower, me + 1 + step).astype(jnp.float32)
        if step < size - 1:
            forward = forward.astype(jnp.bfloat16)
            backward = backward.astype(jnp.bfloat16)
    return jnp.concatenate([forward, backward], axis=0)


def body(sent, queries, keys, values, segments, out_weight, norm_gain):
    n_pipe = lax.axis_size("pipe")
    n_ctx = lax.axis_size("ctx")
    n_tp = lax.axis_size("tp")

    with jax.named_scope("relay"):
        arrived_stream = shifted(sent, "pipe", 1, n_pipe)[0]
        section_index = lax.axis_index("pipe")
        incoming = jnp.where(section_index == 0, sent[0], arrived_stream)

    query_local = queries[0]
    tok_rows = query_local.shape[0]
    kv_heads = keys.shape[2] // HEAD
    query_heads = query_local.shape[1] // HEAD
    group_size = query_heads // kv_heads
    kv_width = kv_heads * HEAD
    scale = HEAD ** (-0.5)
    ctx_index = lax.axis_index("ctx")
    first_pos = ctx_index * tok_rows

    back = min(n_ctx - 1, -(-(LONGEST_DOC - 1) // tok_rows))

    with jax.named_scope("kv_exchange"):
        own_docs = segments[0]
        doc_row = jnp.zeros((16, 2 * kv_width), jnp.bfloat16)
        doc_row = doc_row.at[0, :tok_rows].set(own_docs.astype(jnp.bfloat16))
        packed = jnp.concatenate(
            [jnp.concatenate([keys[0], values[0]], axis=1), doc_row], axis=0
        )
        core = lax.rem(ctx_index, 2)
        chip_back = -(-back // 2)
        near = [shifted(packed, "ctx", 2 * d, n_ctx) for d in (3, 2, 1)]
        oldest = shifted(packed, "ctx", 2 * chip_back, n_ctx)
        quad = jnp.stack(near + [packed])
        mine = [oldest[None]]
        reach = 4
        while reach < chip_back:
            mine.append(shifted(quad, "ctx", 2 * reach, n_ctx))
            reach += 4
        mine.append(quad)
        mine = jnp.concatenate(mine, axis=0)
        assert mine.shape[0] == chip_back + 1
        partner = lax.ppermute(mine, "ctx", [(i, i ^ 1) for i in range(n_ctx)])
        stacked = jnp.concatenate([mine, partner], axis=0)
        chip_of_block = jnp.concatenate([jnp.arange(-chip_back, 1, dtype=jnp.int32)] * 2)
        core_of_block = jnp.concatenate(
            [jnp.full((chip_back + 1,), 0, jnp.int32), jnp.full((chip_back + 1,), 1, jnp.int32)]
        )
        block_index = (ctx_index - core) + 2 * chip_of_block + lax.rem(core + core_of_block, 2)

    with jax.named_scope("attention"):
        n_blocks = stacked.shape[0]
        n_keys = n_blocks * tok_rows
        key_rows = stacked[:, :tok_rows, :kv_width].reshape(n_keys, kv_heads, HEAD)
        value_rows = stacked[:, :tok_rows, kv_width:].reshape(n_keys, kv_heads, HEAD)
        key_docs = stacked[:, tok_rows, :tok_rows].reshape(n_keys).astype(jnp.int32)
        key_pos = (
            block_index[:, None] * tok_rows + jnp.arange(tok_rows, dtype=jnp.int32)[None, :]
        ).reshape(n_keys)
        query_pos = first_pos + jnp.arange(tok_rows, dtype=jnp.int32)
        allowed = (
            (key_pos[None, :] <= query_pos[:, None])
            & (key_pos[None, :] >= 0)
            & (key_docs[None, :] == own_docs[:, None])
        )
        query_split = query_local.reshape(tok_rows, kv_heads, group_size, HEAD)
        scores = (
            jnp.einsum("tkgd,nkd->kgtn", query_split, key_rows, preferred_element_type=jnp.float32)
            * scale
        )
        masked = jnp.where(allowed, scores, -1e30)
        top = jnp.max(masked, axis=-1, keepdims=True)
        weights = jnp.where(allowed, jnp.exp(masked - top), 0.0)
        denom = jnp.sum(weights, axis=-1)
        mixed = jnp.einsum(
            "kgtn,nkd->tkgd",
            weights.astype(jnp.bfloat16),
            value_rows,
            preferred_element_type=jnp.float32,
        )
        attention = (mixed / denom.transpose(2, 0, 1)[..., None]).reshape(
            tok_rows, query_heads * HEAD
        ).astype(jnp.bfloat16)

    with jax.named_scope("projection"):
        projected = jnp.dot(attention, out_weight[0], preferred_element_type=jnp.float32)
        branch = ring_reduce_scatter(projected.astype(jnp.bfloat16), n_tp)

    with jax.named_scope("norm"):
        square_sum = jnp.sum(branch * branch, axis=-1)
        mean_square = lax.psum(square_sum, "tp") / D
        normed = branch * lax.rsqrt(mean_square + 1e-06)[:, None] * norm_gain[0][None, :]
        emitted = (incoming.astype(jnp.float32) + normed).astype(jnp.bfloat16)
    return emitted[None]


def solution(mesh):
    return jax.shard_map(
        body,
        mesh=mesh,
        in_specs=(
            P("pipe", "ctx", "tp"),
            P("pipe", "ctx", "tp"),
            P("pipe", "ctx", "tp"),
            P("pipe", "ctx", "tp"),
            P("pipe", "ctx"),
            P("pipe", "tp", None),
            P("pipe", "tp"),
        ),
        out_specs=P("pipe", "ctx", "tp"),
        check_vma=False,
    )
```

```python
import jax
import jax.numpy as jnp
from jax import lax
from jax.experimental import pallas as pl
from jax.experimental.pallas import tpu as pltpu
from jax.sharding import PartitionSpec as P

D = 5376
HEAD = 128
LONGEST_DOC = 2048


def shifted(block, axis, distance, size):
    route = [(i, i + distance) for i in range(size) if i + distance < size]
    return lax.ppermute(block, axis, route)


def rotated(block, axis, distance, size):
    route = [(i, (i + distance) % size) for i in range(size)]
    return lax.ppermute(block, axis, route)


def ring_reduce_scatter(product, size):
    rows, width = product.shape
    cols = width // size
    half = rows // 2
    me = lax.axis_index("tp")

    def chunk(part, index):
        start = (lax.rem(index + 2 * size, size)) * cols
        return lax.dynamic_slice_in_dim(part, start, cols, axis=1)

    upper, lower = product[:half], product[half:]
    forward = chunk(upper, me - 1)
    backward = chunk(lower, me + 1)
    for step in range(1, size):
        forward = rotated(forward, "tp", 1, size)
        backward = rotated(backward, "tp", size - 1, size)
        forward = forward.astype(jnp.float32) + chunk(upper, me - 1 - step).astype(jnp.float32)
        backward = backward.astype(jnp.float32) + chunk(lower, me + 1 + step).astype(jnp.float32)
        if step < size - 1:
            forward = forward.astype(jnp.bfloat16)
            backward = backward.astype(jnp.bfloat16)
    return jnp.concatenate([forward, backward], axis=0)


def attention_kernel(counts, heads, group_size, scale, *refs):
    q_ref, qpos_ref, qdoc_ref, kpos_ref = refs[:4]
    pieces = refs[4:4 + len(counts)]
    out_ref, s_ref, w_ref = refs[4 + len(counts):]
    tok = q_ref.shape[0]
    kv_width = pieces[0].shape[-1] // 2
    qpos = qpos_ref[...]
    qdoc = qdoc_ref[...].astype(jnp.float32)
    queries = [q_ref[:, h * HEAD:(h + 1) * HEAD] for h in range(heads)]
    column = 0
    for piece, count in zip(pieces, counts):
        for b in range(count):
            lanes = pl.ds(column * tok, tok)
            kpos = kpos_ref[:, lanes]
            kdoc = piece[b, tok:tok + 1, 0:tok].astype(jnp.float32)
            allowed = (kpos <= qpos) & (kpos >= 0) & (kdoc == qdoc)
            for h in range(heads):
                k = h // group_size
                key = piece[b, 0:tok, k * HEAD:(k + 1) * HEAD]
                score = lax.dot_general(
                    queries[h], key, (((1,), (1,)), ((), ())),
                    preferred_element_type=jnp.float32,
                ) * scale
                s_ref[h, :, lanes] = jnp.where(allowed, score, -1e30)
            column += 1
    for h in range(heads):
        k = h // group_size
        masked = s_ref[h]
        top = jnp.max(masked, axis=1, keepdims=True)
        weights = jnp.exp(masked - top)
        denom = jnp.sum(weights, axis=1, keepdims=True)
        w_ref[...] = weights.astype(jnp.bfloat16)
        acc = jnp.zeros((tok, HEAD), jnp.float32)
        column = 0
        for piece, count in zip(pieces, counts):
            for b in range(count):
                value = piece[b, 0:tok, kv_width + k * HEAD:kv_width + (k + 1) * HEAD]
                acc = acc + jnp.dot(
                    w_ref[:, pl.ds(column * tok, tok)], value,
                    preferred_element_type=jnp.float32,
                )
                column += 1
        out_ref[:, h * HEAD:(h + 1) * HEAD] = (acc / denom).astype(out_ref.dtype)


def attend(query, query_pos, query_docs, key_pos, pieces, group_size, scale):
    tok, width = query.shape
    heads = width // HEAD
    counts = tuple(p.shape[0] for p in pieces)
    n_keys = sum(counts) * tok
    vmem = pl.BlockSpec(memory_space=pltpu.VMEM)
    flops = 4 * heads * tok * n_keys * HEAD
    nbytes = sum(p.size * 2 for p in pieces) + 2 * query.size * 2
    return pl.pallas_call(
        lambda *refs: attention_kernel(counts, heads, group_size, scale, *refs),
        out_shape=jax.ShapeDtypeStruct((tok, width), jnp.bfloat16),
        in_specs=[vmem] * (4 + len(pieces)),
        out_specs=vmem,
        scratch_shapes=[
            pltpu.VMEM((heads, tok, n_keys), jnp.float32),
            pltpu.VMEM((tok, n_keys), jnp.bfloat16),
        ],
        compiler_params=pltpu.CompilerParams(vmem_limit_bytes=48 * 1024 * 1024),
        cost_estimate=pl.CostEstimate(
            flops=flops, transcendentals=heads * tok * n_keys, bytes_accessed=nbytes
        ),
        name="window_attention",
    )(query, query_pos[:, None], query_docs[:, None], key_pos[None, :], *pieces)


def body(sent, queries, keys, values, segments, out_weight, norm_gain):
    n_pipe = lax.axis_size("pipe")
    n_ctx = lax.axis_size("ctx")
    n_tp = lax.axis_size("tp")

    with jax.named_scope("relay"):
        arrived_stream = shifted(sent, "pipe", 1, n_pipe)[0]
        section_index = lax.axis_index("pipe")
        incoming = jnp.where(section_index == 0, sent[0], arrived_stream)

    query_local = queries[0]
    tok_rows = query_local.shape[0]
    kv_heads = keys.shape[2] // HEAD
    query_heads = query_local.shape[1] // HEAD
    group_size = query_heads // kv_heads
    kv_width = kv_heads * HEAD
    scale = HEAD ** (-0.5)
    ctx_index = lax.axis_index("ctx")
    first_pos = ctx_index * tok_rows

    back = min(n_ctx - 1, -(-(LONGEST_DOC - 1) // tok_rows))

    with jax.named_scope("kv_exchange"):
        own_docs = segments[0]
        doc_row = jnp.zeros((16, 2 * kv_width), jnp.bfloat16)
        doc_row = doc_row.at[0, :tok_rows].set(own_docs.astype(jnp.bfloat16))
        packed = jnp.concatenate(
            [jnp.concatenate([keys[0], values[0]], axis=1), doc_row], axis=0
        )
        core = lax.rem(ctx_index, 2)
        chip_back = -(-back // 2)
        near = [shifted(packed, "ctx", 2 * d, n_ctx) for d in (3, 2, 1)]
        oldest = shifted(packed, "ctx", 2 * chip_back, n_ctx)
        quad = jnp.stack(near + [packed])
        swap = [(i, i ^ 1) for i in range(n_ctx)]
        oldest = oldest[None]
        mine = [oldest]
        reach = 4
        while reach < chip_back:
            mine.append(shifted(quad, "ctx", 2 * reach, n_ctx))
            reach += 4
        mine.append(quad)
        assert sum(p.shape[0] for p in mine) == chip_back + 1
        theirs = [lax.ppermute(p, "ctx", swap) for p in mine]
        chip_of_block = jnp.concatenate([jnp.arange(-chip_back, 1, dtype=jnp.int32)] * 2)
        core_of_block = jnp.concatenate(
            [jnp.full((chip_back + 1,), 0, jnp.int32), jnp.full((chip_back + 1,), 1, jnp.int32)]
        )
        block_index = (ctx_index - core) + 2 * chip_of_block + lax.rem(core + core_of_block, 2)

    with jax.named_scope("attention"):
        key_pos = (
            block_index[:, None] * tok_rows + jnp.arange(tok_rows, dtype=jnp.int32)[None, :]
        ).reshape(-1)
        query_pos = first_pos + jnp.arange(tok_rows, dtype=jnp.int32)
        attention = attend(
            query_local, query_pos, own_docs, key_pos, mine + theirs, group_size, scale
        )

    with jax.named_scope("projection"):
        projected = jnp.dot(attention, out_weight[0], preferred_element_type=jnp.float32)
        branch = ring_reduce_scatter(projected.astype(jnp.bfloat16), n_tp)

    with jax.named_scope("norm"):
        square_sum = jnp.sum(branch * branch, axis=-1)
        mean_square = lax.psum(square_sum, "tp") / D
        normed = branch * lax.rsqrt(mean_square + 1e-06)[:, None] * norm_gain[0][None, :]
        emitted = (incoming.astype(jnp.float32) + normed).astype(jnp.bfloat16)
    return emitted[None]


def solution(mesh):
    return jax.shard_map(
        body,
        mesh=mesh,
        in_specs=(
            P("pipe", "ctx", "tp"),
            P("pipe", "ctx", "tp"),
            P("pipe", "ctx", "tp"),
            P("pipe", "ctx", "tp"),
            P("pipe", "ctx"),
            P("pipe", "tp", None),
            P("pipe", "tp"),
        ),
        out_specs=P("pipe", "ctx", "tp"),
        check_vma=False,
    )
```

```python
import jax
import jax.numpy as jnp
from jax import lax
from jax.experimental import pallas as pl
from jax.experimental.pallas import tpu as pltpu
from jax.sharding import PartitionSpec as P

D = 5376
HEAD = 128
LONGEST_DOC = 2048


def shifted(block, axis, distance, size):
    route = [(i, i + distance) for i in range(size) if i + distance < size]
    return lax.ppermute(block, axis, route)


def rotated(block, axis, distance, size):
    route = [(i, (i + distance) % size) for i in range(size)]
    return lax.ppermute(block, axis, route)


def ring_reduce_scatter(product, size, splits=2):
    rows, width = product.shape
    cols = width // size
    slab = rows // (2 * splits)
    me = lax.axis_index("tp")

    def chunk(part, index):
        start = (lax.rem(index + 2 * size, size)) * cols
        return lax.dynamic_slice_in_dim(part, start, cols, axis=1)

    parts = [product[i * slab:(i + 1) * slab] for i in range(2 * splits)]
    ways = [1] * splits + [-1] * splits
    moving = [chunk(p, me - w) for p, w in zip(parts, ways)]
    for step in range(1, size):
        moving = [rotated(m, "tp", w % size, size) for m, w in zip(moving, ways)]
        moving = [
            m.astype(jnp.float32) + chunk(p, me - w * (1 + step)).astype(jnp.float32)
            for m, p, w in zip(moving, parts, ways)
        ]
        if step < size - 1:
            moving = [m.astype(jnp.bfloat16) for m in moving]
    return jnp.concatenate(moving, axis=0)

def attention_kernel(counts, heads, group_size, scale, *refs):
    q_ref, qpos_ref, qdoc_ref, kpos_ref = refs[:4]
    pieces = refs[4:4 + len(counts)]
    out_ref, s_ref, w_ref = refs[4 + len(counts):]
    tok = q_ref.shape[0]
    kv_width = pieces[0].shape[-1] // 2
    qpos = qpos_ref[...]
    qdoc = qdoc_ref[...].astype(jnp.float32)
    queries = [q_ref[:, h * HEAD:(h + 1) * HEAD] for h in range(heads)]
    column = 0
    for piece, count in zip(pieces, counts):
        for b in range(count):
            lanes = pl.ds(column * tok, tok)
            kpos = kpos_ref[:, lanes]
            kdoc = piece[b, tok:tok + 1, 0:tok].astype(jnp.float32)
            allowed = (kpos <= qpos) & (kpos >= 0) & (kdoc == qdoc)
            for h in range(heads):
                k = h // group_size
                key = piece[b, 0:tok, k * HEAD:(k + 1) * HEAD]
                score = lax.dot_general(
                    queries[h], key, (((1,), (1,)), ((), ())),
                    preferred_element_type=jnp.float32,
                ) * scale
                s_ref[h, :, lanes] = jnp.where(allowed, score, -1e30)
            column += 1
    for h in range(heads):
        k = h // group_size
        masked = s_ref[h]
        top = jnp.max(masked, axis=1, keepdims=True)
        weights = jnp.exp(masked - top)
        denom = jnp.sum(weights, axis=1, keepdims=True)
        w_ref[...] = weights.astype(jnp.bfloat16)
        acc = jnp.zeros((tok, HEAD), jnp.float32)
        column = 0
        for piece, count in zip(pieces, counts):
            for b in range(count):
                value = piece[b, 0:tok, kv_width + k * HEAD:kv_width + (k + 1) * HEAD]
                acc = acc + jnp.dot(
                    w_ref[:, pl.ds(column * tok, tok)], value,
                    preferred_element_type=jnp.float32,
                )
                column += 1
        out_ref[:, h * HEAD:(h + 1) * HEAD] = (acc / denom).astype(out_ref.dtype)


def attend(query, query_pos, query_docs, key_pos, pieces, group_size, scale):
    tok, width = query.shape
    heads = width // HEAD
    counts = tuple(p.shape[0] for p in pieces)
    n_keys = sum(counts) * tok
    vmem = pl.BlockSpec(memory_space=pltpu.VMEM)
    flops = 4 * heads * tok * n_keys * HEAD
    nbytes = sum(p.size * 2 for p in pieces) + 2 * query.size * 2
    return pl.pallas_call(
        lambda *refs: attention_kernel(counts, heads, group_size, scale, *refs),
        out_shape=jax.ShapeDtypeStruct((tok, width), jnp.bfloat16),
        in_specs=[vmem] * (4 + len(pieces)),
        out_specs=vmem,
        scratch_shapes=[
            pltpu.VMEM((heads, tok, n_keys), jnp.float32),
            pltpu.VMEM((tok, n_keys), jnp.bfloat16),
        ],
        compiler_params=pltpu.CompilerParams(vmem_limit_bytes=48 * 1024 * 1024),
        cost_estimate=pl.CostEstimate(
            flops=flops, transcendentals=heads * tok * n_keys, bytes_accessed=nbytes
        ),
        name="window_attention",
    )(query, query_pos[:, None], query_docs[:, None], key_pos[None, :], *pieces)


def body(sent, queries, keys, values, segments, out_weight, norm_gain):
    n_pipe = lax.axis_size("pipe")
    n_ctx = lax.axis_size("ctx")
    n_tp = lax.axis_size("tp")

    with jax.named_scope("relay"):
        arrived_stream = shifted(sent, "pipe", 1, n_pipe)[0]
        section_index = lax.axis_index("pipe")
        incoming = jnp.where(section_index == 0, sent[0], arrived_stream)

    query_local = queries[0]
    tok_rows = query_local.shape[0]
    kv_heads = keys.shape[2] // HEAD
    query_heads = query_local.shape[1] // HEAD
    group_size = query_heads // kv_heads
    kv_width = kv_heads * HEAD
    scale = HEAD ** (-0.5)
    ctx_index = lax.axis_index("ctx")
    first_pos = ctx_index * tok_rows

    back = min(n_ctx - 1, -(-(LONGEST_DOC - 1) // tok_rows))

    with jax.named_scope("kv_exchange"):
        own_docs = segments[0]
        doc_row = jnp.zeros((16, 2 * kv_width), jnp.bfloat16)
        doc_row = doc_row.at[0, :tok_rows].set(own_docs.astype(jnp.bfloat16))
        packed = jnp.concatenate(
            [jnp.concatenate([keys[0], values[0]], axis=1), doc_row], axis=0
        )
        core = lax.rem(ctx_index, 2)
        chip_back = -(-back // 2)
        near = [shifted(packed, "ctx", 2 * d, n_ctx) for d in (3, 2, 1)]
        oldest = shifted(packed, "ctx", 2 * chip_back, n_ctx)
        quad = jnp.stack(near + [packed])
        swap = [(i, i ^ 1) for i in range(n_ctx)]
        oldest = oldest[None]
        mine = [oldest]
        reach = 4
        while reach < chip_back:
            mine.append(shifted(quad, "ctx", 2 * reach, n_ctx))
            reach += 4
        mine.append(quad)
        assert sum(p.shape[0] for p in mine) == chip_back + 1
        theirs = [lax.ppermute(p, "ctx", swap) for p in mine]
        chip_of_block = jnp.concatenate([jnp.arange(-chip_back, 1, dtype=jnp.int32)] * 2)
        core_of_block = jnp.concatenate(
            [jnp.full((chip_back + 1,), 0, jnp.int32), jnp.full((chip_back + 1,), 1, jnp.int32)]
        )
        block_index = (ctx_index - core) + 2 * chip_of_block + lax.rem(core + core_of_block, 2)

    with jax.named_scope("attention"):
        key_pos = (
            block_index[:, None] * tok_rows + jnp.arange(tok_rows, dtype=jnp.int32)[None, :]
        ).reshape(-1)
        query_pos = first_pos + jnp.arange(tok_rows, dtype=jnp.int32)
        attention = attend(
            query_local, query_pos, own_docs, key_pos, mine + theirs, group_size, scale
        )

    with jax.named_scope("projection"):
        projected = jnp.dot(attention, out_weight[0], preferred_element_type=jnp.float32)
        branch = ring_reduce_scatter(projected.astype(jnp.bfloat16), n_tp)

    with jax.named_scope("norm"):
        square_sum = jnp.sum(branch * branch, axis=-1)
        mean_square = lax.psum(square_sum, "tp") / D
        normed = branch * lax.rsqrt(mean_square + 1e-06)[:, None] * norm_gain[0][None, :]
        emitted = (incoming.astype(jnp.float32) + normed).astype(jnp.bfloat16)
    return emitted[None]


def solution(mesh):
    return jax.shard_map(
        body,
        mesh=mesh,
        in_specs=(
            P("pipe", "ctx", "tp"),
            P("pipe", "ctx", "tp"),
            P("pipe", "ctx", "tp"),
            P("pipe", "ctx", "tp"),
            P("pipe", "ctx"),
            P("pipe", "tp", None),
            P("pipe", "tp"),
        ),
        out_specs=P("pipe", "ctx", "tp"),
        check_vma=False,
    )
```

```python
import jax
import jax.numpy as jnp
from jax import lax
from jax.experimental import pallas as pl
from jax.experimental.pallas import tpu as pltpu
from jax.sharding import PartitionSpec as P

D = 5376
HEAD = 128
LONGEST_DOC = 2048


def shifted(block, axis, distance, size):
    route = [(i, i + distance) for i in range(size) if i + distance < size]
    return lax.ppermute(block, axis, route)


def rotated(block, axis, distance, size):
    route = [(i, (i + distance) % size) for i in range(size)]
    return lax.ppermute(block, axis, route)


def ring_reduce_scatter(product, size, splits=1):
    rows, width = product.shape
    cols = width // size
    slab = rows // (2 * splits)
    me = lax.axis_index("tp")

    def chunk(part, index):
        start = (lax.rem(index + 2 * size, size)) * cols
        return lax.dynamic_slice_in_dim(part, start, cols, axis=1)

    parts = [product[i * slab:(i + 1) * slab] for i in range(2 * splits)]
    ways = [1] * splits + [-1] * splits
    moving = [chunk(p, me - w) for p, w in zip(parts, ways)]
    for step in range(1, size):
        moving = [rotated(m, "tp", w % size, size) for m, w in zip(moving, ways)]
        moving = [
            m.astype(jnp.float32) + chunk(p, me - w * (1 + step)).astype(jnp.float32)
            for m, p, w in zip(moving, parts, ways)
        ]
        if step < size - 1:
            moving = [m.astype(jnp.bfloat16) for m in moving]
    return jnp.concatenate(moving, axis=0)

def attention_kernel(counts, heads, group_size, scale, *refs):
    q_ref, qpos_ref, qdoc_ref, kpos_ref = refs[:4]
    pieces = refs[4:4 + len(counts)]
    out_ref, s_ref, w_ref = refs[4 + len(counts):]
    tok = q_ref.shape[0]
    kv_width = pieces[0].shape[-1] // 2
    qpos = qpos_ref[...]
    qdoc = qdoc_ref[...].astype(jnp.float32)
    queries = [q_ref[:, h * HEAD:(h + 1) * HEAD] for h in range(heads)]
    column = 0
    for piece, count in zip(pieces, counts):
        for b in range(count):
            lanes = pl.ds(column * tok, tok)
            kpos = kpos_ref[:, lanes]
            kdoc = piece[b, tok:tok + 1, 0:tok].astype(jnp.float32)
            allowed = (kpos <= qpos) & (kpos >= 0) & (kdoc == qdoc)
            for h in range(heads):
                k = h // group_size
                key = piece[b, 0:tok, k * HEAD:(k + 1) * HEAD]
                score = lax.dot_general(
                    queries[h], key, (((1,), (1,)), ((), ())),
                    preferred_element_type=jnp.float32,
                ) * scale
                s_ref[h, :, lanes] = jnp.where(allowed, score, -1e30)
            column += 1
    for h in range(heads):
        k = h // group_size
        masked = s_ref[h]
        top = jnp.max(masked, axis=1, keepdims=True)
        weights = jnp.exp(masked - top)
        denom = jnp.sum(weights, axis=1, keepdims=True)
        w_ref[...] = weights.astype(jnp.bfloat16)
        acc = jnp.zeros((tok, HEAD), jnp.float32)
        column = 0
        for piece, count in zip(pieces, counts):
            for b in range(count):
                value = piece[b, 0:tok, kv_width + k * HEAD:kv_width + (k + 1) * HEAD]
                acc = acc + jnp.dot(
                    w_ref[:, pl.ds(column * tok, tok)], value,
                    preferred_element_type=jnp.float32,
                )
                column += 1
        out_ref[:, h * HEAD:(h + 1) * HEAD] = (acc / denom).astype(out_ref.dtype)


def attend(query, query_pos, query_docs, key_pos, pieces, group_size, scale):
    tok, width = query.shape
    heads = width // HEAD
    counts = tuple(p.shape[0] for p in pieces)
    n_keys = sum(counts) * tok
    vmem = pl.BlockSpec(memory_space=pltpu.VMEM)
    flops = 4 * heads * tok * n_keys * HEAD
    nbytes = sum(p.size * 2 for p in pieces) + 2 * query.size * 2
    return pl.pallas_call(
        lambda *refs: attention_kernel(counts, heads, group_size, scale, *refs),
        out_shape=jax.ShapeDtypeStruct((tok, width), jnp.bfloat16),
        in_specs=[vmem] * (4 + len(pieces)),
        out_specs=vmem,
        scratch_shapes=[
            pltpu.VMEM((heads, tok, n_keys), jnp.float32),
            pltpu.VMEM((tok, n_keys), jnp.bfloat16),
        ],
        compiler_params=pltpu.CompilerParams(vmem_limit_bytes=48 * 1024 * 1024),
        cost_estimate=pl.CostEstimate(
            flops=flops, transcendentals=heads * tok * n_keys, bytes_accessed=nbytes
        ),
        name="window_attention",
    )(query, query_pos[:, None], query_docs[:, None], key_pos[None, :], *pieces)


def body(sent, queries, keys, values, segments, out_weight, norm_gain):
    n_pipe = lax.axis_size("pipe")
    n_ctx = lax.axis_size("ctx")
    n_tp = lax.axis_size("tp")

    with jax.named_scope("relay"):
        arrived_stream = shifted(sent, "pipe", 1, n_pipe)[0]
        section_index = lax.axis_index("pipe")
        incoming = jnp.where(section_index == 0, sent[0], arrived_stream)

    query_local = queries[0]
    tok_rows = query_local.shape[0]
    kv_heads = keys.shape[2] // HEAD
    query_heads = query_local.shape[1] // HEAD
    group_size = query_heads // kv_heads
    kv_width = kv_heads * HEAD
    scale = HEAD ** (-0.5)
    ctx_index = lax.axis_index("ctx")
    first_pos = ctx_index * tok_rows

    back = min(n_ctx - 1, -(-(LONGEST_DOC - 1) // tok_rows))

    with jax.named_scope("kv_exchange"):
        own_docs = segments[0]
        doc_row = jnp.zeros((16, 2 * kv_width), jnp.bfloat16)
        doc_row = doc_row.at[0, :tok_rows].set(own_docs.astype(jnp.bfloat16))
        packed = jnp.concatenate(
            [jnp.concatenate([keys[0], values[0]], axis=1), doc_row], axis=0
        )
        core = lax.rem(ctx_index, 2)
        chip_back = -(-back // 2)
        fetched = {d: shifted(packed, "ctx", 2 * d, n_ctx) for d in range(chip_back, 0, -1)}
        split = chip_back // 2
        older = jnp.stack([fetched[d] for d in range(chip_back, split, -1)])
        newer = jnp.stack([fetched[d] for d in range(split, 0, -1)] + [packed])
        swap = [(i, i ^ 1) for i in range(n_ctx)]
        mine = [older, newer]
        assert sum(p.shape[0] for p in mine) == chip_back + 1
        theirs = [lax.ppermute(p, "ctx", swap) for p in mine]
        chip_of_block = jnp.concatenate([jnp.arange(-chip_back, 1, dtype=jnp.int32)] * 2)
        core_of_block = jnp.concatenate(
            [jnp.full((chip_back + 1,), 0, jnp.int32), jnp.full((chip_back + 1,), 1, jnp.int32)]
        )
        block_index = (ctx_index - core) + 2 * chip_of_block + lax.rem(core + core_of_block, 2)

    with jax.named_scope("attention"):
        key_pos = (
            block_index[:, None] * tok_rows + jnp.arange(tok_rows, dtype=jnp.int32)[None, :]
        ).reshape(-1)
        query_pos = first_pos + jnp.arange(tok_rows, dtype=jnp.int32)
        attention = attend(
            query_local, query_pos, own_docs, key_pos, mine + theirs, group_size, scale
        )

    with jax.named_scope("projection"):
        projected = jnp.dot(attention, out_weight[0], preferred_element_type=jnp.float32)
        branch = ring_reduce_scatter(projected.astype(jnp.bfloat16), n_tp)

    with jax.named_scope("norm"):
        square_sum = jnp.sum(branch * branch, axis=-1)
        mean_square = lax.psum(square_sum, "tp") / D
        normed = branch * lax.rsqrt(mean_square + 1e-06)[:, None] * norm_gain[0][None, :]
        emitted = (incoming.astype(jnp.float32) + normed).astype(jnp.bfloat16)
    return emitted[None]


def solution(mesh):
    return jax.shard_map(
        body,
        mesh=mesh,
        in_specs=(
            P("pipe", "ctx", "tp"),
            P("pipe", "ctx", "tp"),
            P("pipe", "ctx", "tp"),
            P("pipe", "ctx", "tp"),
            P("pipe", "ctx"),
            P("pipe", "tp", None),
            P("pipe", "tp"),
        ),
        out_specs=P("pipe", "ctx", "tp"),
        check_vma=False,
    )
```

```python
import jax
import jax.numpy as jnp
from jax import lax
from jax.experimental import pallas as pl
from jax.experimental.pallas import tpu as pltpu
from jax.sharding import PartitionSpec as P

D = 5376
HEAD = 128
LONGEST_DOC = 2048


def shifted(block, axis, distance, size):
    route = [(i, i + distance) for i in range(size) if i + distance < size]
    return lax.ppermute(block, axis, route)


def rotated(block, axis, distance, size):
    route = [(i, (i + distance) % size) for i in range(size)]
    return lax.ppermute(block, axis, route)


def ring_reduce_scatter(product, size, splits=1):
    rows, width = product.shape
    cols = width // size
    slab = rows // (2 * splits)
    me = lax.axis_index("tp")

    def chunk(part, index):
        start = (lax.rem(index + 2 * size, size)) * cols
        return lax.dynamic_slice_in_dim(part, start, cols, axis=1)

    parts = [product[i * slab:(i + 1) * slab] for i in range(2 * splits)]
    ways = [1] * splits + [-1] * splits
    moving = [chunk(p, me - w) for p, w in zip(parts, ways)]
    for step in range(1, size):
        moving = [rotated(m, "tp", w % size, size) for m, w in zip(moving, ways)]
        moving = [
            m.astype(jnp.float32) + chunk(p, me - w * (1 + step)).astype(jnp.float32)
            for m, p, w in zip(moving, parts, ways)
        ]
        if step < size - 1:
            moving = [m.astype(jnp.bfloat16) for m in moving]
    return jnp.concatenate(moving, axis=0)

def attention_kernel(counts, heads, group_size, scale, *refs):
    q_ref, qpos_ref, qdoc_ref, kpos_ref = refs[:4]
    pieces = refs[4:4 + len(counts)]
    out_ref, s_ref, w_ref = refs[4 + len(counts):]
    tok = q_ref.shape[0]
    kv_width = pieces[0].shape[-1] // 2
    qpos = qpos_ref[...]
    qdoc = qdoc_ref[...].astype(jnp.float32)
    queries = [q_ref[:, h * HEAD:(h + 1) * HEAD] for h in range(heads)]
    column = 0
    for piece, count in zip(pieces, counts):
        for b in range(count):
            lanes = pl.ds(column * tok, tok)
            kpos = kpos_ref[:, lanes]
            kdoc = piece[b, tok:tok + 1, 0:tok].astype(jnp.float32)
            allowed = (kpos <= qpos) & (kpos >= 0) & (kdoc == qdoc)
            for h in range(heads):
                k = h // group_size
                key = piece[b, 0:tok, k * HEAD:(k + 1) * HEAD]
                score = lax.dot_general(
                    queries[h], key, (((1,), (1,)), ((), ())),
                    preferred_element_type=jnp.float32,
                ) * scale
                s_ref[h, :, lanes] = jnp.where(allowed, score, -1e30)
            column += 1
    for h in range(heads):
        k = h // group_size
        masked = s_ref[h]
        top = jnp.max(masked, axis=1, keepdims=True)
        weights = jnp.exp(masked - top)
        denom = jnp.sum(weights, axis=1, keepdims=True)
        w_ref[...] = weights.astype(jnp.bfloat16)
        acc = jnp.zeros((tok, HEAD), jnp.float32)
        column = 0
        for piece, count in zip(pieces, counts):
            for b in range(count):
                value = piece[b, 0:tok, kv_width + k * HEAD:kv_width + (k + 1) * HEAD]
                acc = acc + jnp.dot(
                    w_ref[:, pl.ds(column * tok, tok)], value,
                    preferred_element_type=jnp.float32,
                )
                column += 1
        out_ref[:, h * HEAD:(h + 1) * HEAD] = (acc / denom).astype(out_ref.dtype)


def attend(query, query_pos, query_docs, key_pos, pieces, group_size, scale):
    tok, width = query.shape
    heads = width // HEAD
    counts = tuple(p.shape[0] for p in pieces)
    n_keys = sum(counts) * tok
    vmem = pl.BlockSpec(memory_space=pltpu.VMEM)
    flops = 4 * heads * tok * n_keys * HEAD
    nbytes = sum(p.size * 2 for p in pieces) + 2 * query.size * 2
    return pl.pallas_call(
        lambda *refs: attention_kernel(counts, heads, group_size, scale, *refs),
        out_shape=jax.ShapeDtypeStruct((tok, width), jnp.bfloat16),
        in_specs=[vmem] * (4 + len(pieces)),
        out_specs=vmem,
        scratch_shapes=[
            pltpu.VMEM((heads, tok, n_keys), jnp.float32),
            pltpu.VMEM((tok, n_keys), jnp.bfloat16),
        ],
        compiler_params=pltpu.CompilerParams(vmem_limit_bytes=48 * 1024 * 1024),
        cost_estimate=pl.CostEstimate(
            flops=flops, transcendentals=heads * tok * n_keys, bytes_accessed=nbytes
        ),
        name="window_attention",
    )(query, query_pos[:, None], query_docs[:, None], key_pos[None, :], *pieces)


def body(sent, queries, keys, values, segments, out_weight, norm_gain):
    n_pipe = lax.axis_size("pipe")
    n_ctx = lax.axis_size("ctx")
    n_tp = lax.axis_size("tp")


    query_local = queries[0]
    tok_rows = query_local.shape[0]
    kv_heads = keys.shape[2] // HEAD
    query_heads = query_local.shape[1] // HEAD
    group_size = query_heads // kv_heads
    kv_width = kv_heads * HEAD
    scale = HEAD ** (-0.5)
    ctx_index = lax.axis_index("ctx")
    first_pos = ctx_index * tok_rows

    back = min(n_ctx - 1, -(-(LONGEST_DOC - 1) // tok_rows))

    with jax.named_scope("kv_exchange"):
        own_docs = segments[0]
        doc_row = jnp.zeros((16, 2 * kv_width), jnp.bfloat16)
        doc_row = doc_row.at[0, :tok_rows].set(own_docs.astype(jnp.bfloat16))
        packed = jnp.concatenate(
            [jnp.concatenate([keys[0], values[0]], axis=1), doc_row], axis=0
        )
        core = lax.rem(ctx_index, 2)
        chip_back = -(-back // 2)
        fetched = {d: shifted(packed, "ctx", 2 * d, n_ctx) for d in range(chip_back, 0, -1)}
        split = chip_back // 2
        older = jnp.stack([fetched[d] for d in range(chip_back, split, -1)])
        newer = jnp.stack([fetched[d] for d in range(split, 0, -1)] + [packed])
        swap = [(i, i ^ 1) for i in range(n_ctx)]
        mine = [older, newer]
        assert sum(p.shape[0] for p in mine) == chip_back + 1
        theirs = [lax.ppermute(p, "ctx", swap) for p in mine]
        chip_of_block = jnp.concatenate([jnp.arange(-chip_back, 1, dtype=jnp.int32)] * 2)
        core_of_block = jnp.concatenate(
            [jnp.full((chip_back + 1,), 0, jnp.int32), jnp.full((chip_back + 1,), 1, jnp.int32)]
        )
        block_index = (ctx_index - core) + 2 * chip_of_block + lax.rem(core + core_of_block, 2)

    with jax.named_scope("attention"):
        key_pos = (
            block_index[:, None] * tok_rows + jnp.arange(tok_rows, dtype=jnp.int32)[None, :]
        ).reshape(-1)
        query_pos = first_pos + jnp.arange(tok_rows, dtype=jnp.int32)
        attention = attend(
            query_local, query_pos, own_docs, key_pos, mine + theirs, group_size, scale
        )

    with jax.named_scope("relay"):
        late_sent, attention = lax.optimization_barrier((sent, attention))
        arrived_stream = shifted(late_sent, "pipe", 1, n_pipe)[0]
        section_index = lax.axis_index("pipe")
        incoming = jnp.where(section_index == 0, late_sent[0], arrived_stream)

    with jax.named_scope("projection"):
        projected = jnp.dot(attention, out_weight[0], preferred_element_type=jnp.float32)
        branch = ring_reduce_scatter(projected.astype(jnp.bfloat16), n_tp)

    with jax.named_scope("norm"):
        square_sum = jnp.sum(branch * branch, axis=-1)
        mean_square = lax.psum(square_sum, "tp") / D
        normed = branch * lax.rsqrt(mean_square + 1e-06)[:, None] * norm_gain[0][None, :]
        emitted = (incoming.astype(jnp.float32) + normed).astype(jnp.bfloat16)
    return emitted[None]


def solution(mesh):
    return jax.shard_map(
        body,
        mesh=mesh,
        in_specs=(
            P("pipe", "ctx", "tp"),
            P("pipe", "ctx", "tp"),
            P("pipe", "ctx", "tp"),
            P("pipe", "ctx", "tp"),
            P("pipe", "ctx"),
            P("pipe", "tp", None),
            P("pipe", "tp"),
        ),
        out_specs=P("pipe", "ctx", "tp"),
        check_vma=False,
    )
```

```python
import jax
import jax.numpy as jnp
from jax import lax
from jax.experimental import pallas as pl
from jax.experimental.pallas import tpu as pltpu
from jax.sharding import PartitionSpec as P

D = 5376
HEAD = 128
LONGEST_DOC = 2048


def shifted(block, axis, distance, size):
    route = [(i, i + distance) for i in range(size) if i + distance < size]
    return lax.ppermute(block, axis, route)


def rotated(block, axis, distance, size):
    route = [(i, (i + distance) % size) for i in range(size)]
    return lax.ppermute(block, axis, route)


def ring_reduce_scatter(product, size, splits=1):
    rows, width = product.shape
    cols = width // size
    slab = rows // (2 * splits)
    me = lax.axis_index("tp")

    def chunk(part, index):
        start = (lax.rem(index + 2 * size, size)) * cols
        return lax.dynamic_slice_in_dim(part, start, cols, axis=1)

    parts = [product[i * slab:(i + 1) * slab] for i in range(2 * splits)]
    ways = [1] * splits + [-1] * splits
    moving = [chunk(p, me - w) for p, w in zip(parts, ways)]
    for step in range(1, size):
        moving = [rotated(m, "tp", w % size, size) for m, w in zip(moving, ways)]
        moving = [
            m.astype(jnp.float32) + chunk(p, me - w * (1 + step)).astype(jnp.float32)
            for m, p, w in zip(moving, parts, ways)
        ]
        if step < size - 1:
            moving = [m.astype(jnp.bfloat16) for m in moving]
    return jnp.concatenate(moving, axis=0)

def attention_kernel(counts, heads, group_size, scale, *refs):
    q_ref, qpos_ref, qdoc_ref, kpos_ref, proj_ref = refs[:5]
    pieces = refs[5:5 + len(counts)]
    out_ref, s_ref, w_ref, a_ref = refs[5 + len(counts):]
    tok = q_ref.shape[0]
    kv_width = pieces[0].shape[-1] // 2
    qpos = qpos_ref[...]
    qdoc = qdoc_ref[...].astype(jnp.float32)
    queries = [q_ref[:, h * HEAD:(h + 1) * HEAD] for h in range(heads)]
    column = 0
    for piece, count in zip(pieces, counts):
        for b in range(count):
            lanes = pl.ds(column * tok, tok)
            kpos = kpos_ref[:, lanes]
            kdoc = piece[b, tok:tok + 1, 0:tok].astype(jnp.float32)
            allowed = (kpos <= qpos) & (kpos >= 0) & (kdoc == qdoc)
            for h in range(heads):
                k = h // group_size
                key = piece[b, 0:tok, k * HEAD:(k + 1) * HEAD]
                score = lax.dot_general(
                    queries[h], key, (((1,), (1,)), ((), ())),
                    preferred_element_type=jnp.float32,
                ) * scale
                s_ref[h, :, lanes] = jnp.where(allowed, score, -1e30)
            column += 1
    for h in range(heads):
        k = h // group_size
        masked = s_ref[h]
        top = jnp.max(masked, axis=1, keepdims=True)
        weights = jnp.exp(masked - top)
        denom = jnp.sum(weights, axis=1, keepdims=True)
        w_ref[...] = weights.astype(jnp.bfloat16)
        acc = jnp.zeros((tok, HEAD), jnp.float32)
        column = 0
        for piece, count in zip(pieces, counts):
            for b in range(count):
                value = piece[b, 0:tok, kv_width + k * HEAD:kv_width + (k + 1) * HEAD]
                acc = acc + jnp.dot(
                    w_ref[:, pl.ds(column * tok, tok)], value,
                    preferred_element_type=jnp.float32,
                )
                column += 1
        a_ref[:, h * HEAD:(h + 1) * HEAD] = (acc / denom).astype(a_ref.dtype)
    out_ref[...] = jnp.dot(
        a_ref[...], proj_ref[...], preferred_element_type=jnp.float32
    ).astype(out_ref.dtype)


def attend(query, query_pos, query_docs, key_pos, pieces, group_size, scale, weight):
    tok, width = query.shape
    features = weight.shape[1]
    heads = width // HEAD
    counts = tuple(p.shape[0] for p in pieces)
    n_keys = sum(counts) * tok
    vmem = pl.BlockSpec(memory_space=pltpu.VMEM)
    flops = 4 * heads * tok * n_keys * HEAD + 2 * tok * width * features
    nbytes = sum(p.size * 2 for p in pieces) + query.size * 2 + weight.size * 2 + tok * features * 2
    return pl.pallas_call(
        lambda *refs: attention_kernel(counts, heads, group_size, scale, *refs),
        out_shape=jax.ShapeDtypeStruct((tok, features), jnp.bfloat16),
        in_specs=[vmem] * (5 + len(pieces)),
        out_specs=vmem,
        scratch_shapes=[
            pltpu.VMEM((heads, tok, n_keys), jnp.float32),
            pltpu.VMEM((tok, n_keys), jnp.bfloat16),
            pltpu.VMEM((tok, width), jnp.bfloat16),
        ],
        compiler_params=pltpu.CompilerParams(vmem_limit_bytes=48 * 1024 * 1024),
        cost_estimate=pl.CostEstimate(
            flops=flops, transcendentals=heads * tok * n_keys, bytes_accessed=nbytes
        ),
        name="window_attention",
    )(query, query_pos[:, None], query_docs[:, None], key_pos[None, :], weight, *pieces)


def body(sent, queries, keys, values, segments, out_weight, norm_gain):
    n_pipe = lax.axis_size("pipe")
    n_ctx = lax.axis_size("ctx")
    n_tp = lax.axis_size("tp")


    query_local = queries[0]
    tok_rows = query_local.shape[0]
    kv_heads = keys.shape[2] // HEAD
    query_heads = query_local.shape[1] // HEAD
    group_size = query_heads // kv_heads
    kv_width = kv_heads * HEAD
    scale = HEAD ** (-0.5)
    ctx_index = lax.axis_index("ctx")
    first_pos = ctx_index * tok_rows

    back = min(n_ctx - 1, -(-(LONGEST_DOC - 1) // tok_rows))

    with jax.named_scope("kv_exchange"):
        own_docs = segments[0]
        doc_row = jnp.zeros((16, 2 * kv_width), jnp.bfloat16)
        doc_row = doc_row.at[0, :tok_rows].set(own_docs.astype(jnp.bfloat16))
        packed = jnp.concatenate(
            [jnp.concatenate([keys[0], values[0]], axis=1), doc_row], axis=0
        )
        core = lax.rem(ctx_index, 2)
        chip_back = -(-back // 2)
        fetched = {d: shifted(packed, "ctx", 2 * d, n_ctx) for d in range(chip_back, 0, -1)}
        split = chip_back // 2
        older = jnp.stack([fetched[d] for d in range(chip_back, split, -1)])
        newer = jnp.stack([fetched[d] for d in range(split, 0, -1)] + [packed])
        swap = [(i, i ^ 1) for i in range(n_ctx)]
        mine = [older, newer]
        assert sum(p.shape[0] for p in mine) == chip_back + 1
        theirs = [lax.ppermute(p, "ctx", swap) for p in mine]
        chip_of_block = jnp.concatenate([jnp.arange(-chip_back, 1, dtype=jnp.int32)] * 2)
        core_of_block = jnp.concatenate(
            [jnp.full((chip_back + 1,), 0, jnp.int32), jnp.full((chip_back + 1,), 1, jnp.int32)]
        )
        block_index = (ctx_index - core) + 2 * chip_of_block + lax.rem(core + core_of_block, 2)

    with jax.named_scope("attention"):
        key_pos = (
            block_index[:, None] * tok_rows + jnp.arange(tok_rows, dtype=jnp.int32)[None, :]
        ).reshape(-1)
        query_pos = first_pos + jnp.arange(tok_rows, dtype=jnp.int32)
        projected = attend(
            query_local, query_pos, own_docs, key_pos, mine + theirs, group_size, scale,
            out_weight[0],
        )

    with jax.named_scope("relay"):
        late_sent, projected = lax.optimization_barrier((sent, projected))
        arrived_stream = shifted(late_sent, "pipe", 1, n_pipe)[0]
        section_index = lax.axis_index("pipe")
        incoming = jnp.where(section_index == 0, late_sent[0], arrived_stream)

    with jax.named_scope("projection"):
        branch = ring_reduce_scatter(projected, n_tp)

    with jax.named_scope("norm"):
        square_sum = jnp.sum(branch * branch, axis=-1)
        mean_square = lax.psum(square_sum, "tp") / D
        normed = branch * lax.rsqrt(mean_square + 1e-06)[:, None] * norm_gain[0][None, :]
        emitted = (incoming.astype(jnp.float32) + normed).astype(jnp.bfloat16)
    return emitted[None]


def solution(mesh):
    return jax.shard_map(
        body,
        mesh=mesh,
        in_specs=(
            P("pipe", "ctx", "tp"),
            P("pipe", "ctx", "tp"),
            P("pipe", "ctx", "tp"),
            P("pipe", "ctx", "tp"),
            P("pipe", "ctx"),
            P("pipe", "tp", None),
            P("pipe", "tp"),
        ),
        out_specs=P("pipe", "ctx", "tp"),
        check_vma=False,
    )
```

```python
import jax
import jax.numpy as jnp
from jax import lax
from jax.experimental import pallas as pl
from jax.experimental.pallas import tpu as pltpu
from jax.sharding import PartitionSpec as P

D = 5376
HEAD = 128
LONGEST_DOC = 2048


def shifted(block, axis, distance, size):
    route = [(i, i + distance) for i in range(size) if i + distance < size]
    return lax.ppermute(block, axis, route)


def rotated(block, axis, distance, size):
    route = [(i, (i + distance) % size) for i in range(size)]
    return lax.ppermute(block, axis, route)


def ring_reduce_scatter(product, size, splits=1):
    rows, width = product.shape
    cols = width // size
    slab = rows // (2 * splits)
    me = lax.axis_index("tp")

    def chunk(part, index):
        start = (lax.rem(index + 2 * size, size)) * cols
        return lax.dynamic_slice_in_dim(part, start, cols, axis=1)

    parts = [product[i * slab:(i + 1) * slab] for i in range(2 * splits)]
    ways = [1] * splits + [-1] * splits
    moving = [chunk(p, me - w) for p, w in zip(parts, ways)]
    for step in range(1, size):
        moving = [rotated(m, "tp", w % size, size) for m, w in zip(moving, ways)]
        moving = [
            m.astype(jnp.float32) + chunk(p, me - w * (1 + step)).astype(jnp.float32)
            for m, p, w in zip(moving, parts, ways)
        ]
        if step < size - 1:
            moving = [m.astype(jnp.bfloat16) for m in moving]
    return jnp.concatenate(moving, axis=0)

def attention_kernel(counts, heads, group_size, scale, *refs):
    q_ref, qpos_ref, qdoc_ref, kpos_ref, proj_ref = refs[:5]
    pieces = refs[5:5 + len(counts)]
    out_ref, s_ref, w_ref, a_ref, weight_vmem, weight_sem = refs[5 + len(counts):]
    weight_copy = pltpu.make_async_copy(proj_ref, weight_vmem, weight_sem)
    weight_copy.start()
    tok = q_ref.shape[0]
    kv_width = pieces[0].shape[-1] // 2
    qpos = qpos_ref[...]
    qdoc = qdoc_ref[...].astype(jnp.float32)
    queries = [q_ref[:, h * HEAD:(h + 1) * HEAD] for h in range(heads)]
    column = 0
    for piece, count in zip(pieces, counts):
        for b in range(count):
            lanes = pl.ds(column * tok, tok)
            kpos = kpos_ref[:, lanes]
            kdoc = piece[b, tok:tok + 1, 0:tok].astype(jnp.float32)
            allowed = (kpos <= qpos) & (kpos >= 0) & (kdoc == qdoc)
            for h in range(heads):
                k = h // group_size
                key = piece[b, 0:tok, k * HEAD:(k + 1) * HEAD]
                score = lax.dot_general(
                    queries[h], key, (((1,), (1,)), ((), ())),
                    preferred_element_type=jnp.float32,
                ) * scale
                s_ref[h, :, lanes] = jnp.where(allowed, score, -1e30)
            column += 1
    for h in range(heads):
        k = h // group_size
        masked = s_ref[h]
        top = jnp.max(masked, axis=1, keepdims=True)
        weights = jnp.exp(masked - top)
        denom = jnp.sum(weights, axis=1, keepdims=True)
        w_ref[...] = weights.astype(jnp.bfloat16)
        acc = jnp.zeros((tok, HEAD), jnp.float32)
        column = 0
        for piece, count in zip(pieces, counts):
            for b in range(count):
                value = piece[b, 0:tok, kv_width + k * HEAD:kv_width + (k + 1) * HEAD]
                acc = acc + jnp.dot(
                    w_ref[:, pl.ds(column * tok, tok)], value,
                    preferred_element_type=jnp.float32,
                )
                column += 1
        a_ref[:, h * HEAD:(h + 1) * HEAD] = (acc / denom).astype(a_ref.dtype)
    weight_copy.wait()
    out_ref[...] = jnp.dot(
        a_ref[...], weight_vmem[...], preferred_element_type=jnp.float32
    ).astype(out_ref.dtype)


def attend(query, query_pos, query_docs, key_pos, pieces, group_size, scale, weight):
    tok, width = query.shape
    features = weight.shape[1]
    heads = width // HEAD
    counts = tuple(p.shape[0] for p in pieces)
    n_keys = sum(counts) * tok
    vmem = pl.BlockSpec(memory_space=pltpu.VMEM)
    flops = 4 * heads * tok * n_keys * HEAD + 2 * tok * width * features
    nbytes = sum(p.size * 2 for p in pieces) + query.size * 2 + weight.size * 2 + tok * features * 2
    return pl.pallas_call(
        lambda *refs: attention_kernel(counts, heads, group_size, scale, *refs),
        out_shape=jax.ShapeDtypeStruct((tok, features), jnp.bfloat16),
        in_specs=[vmem] * 4 + [pl.BlockSpec(memory_space=pl.ANY)] + [vmem] * len(pieces),
        out_specs=vmem,
        scratch_shapes=[
            pltpu.VMEM((heads, tok, n_keys), jnp.float32),
            pltpu.VMEM((tok, n_keys), jnp.bfloat16),
            pltpu.VMEM((tok, width), jnp.bfloat16),
            pltpu.VMEM(weight.shape, weight.dtype),
            pltpu.SemaphoreType.DMA(()),
        ],
        compiler_params=pltpu.CompilerParams(vmem_limit_bytes=48 * 1024 * 1024),
        cost_estimate=pl.CostEstimate(
            flops=flops, transcendentals=heads * tok * n_keys, bytes_accessed=nbytes
        ),
        name="window_attention",
    )(query, query_pos[:, None], query_docs[:, None], key_pos[None, :], weight, *pieces)


def body(sent, queries, keys, values, segments, out_weight, norm_gain):
    n_pipe = lax.axis_size("pipe")
    n_ctx = lax.axis_size("ctx")
    n_tp = lax.axis_size("tp")


    query_local = queries[0]
    tok_rows = query_local.shape[0]
    kv_heads = keys.shape[2] // HEAD
    query_heads = query_local.shape[1] // HEAD
    group_size = query_heads // kv_heads
    kv_width = kv_heads * HEAD
    scale = HEAD ** (-0.5)
    ctx_index = lax.axis_index("ctx")
    first_pos = ctx_index * tok_rows

    back = min(n_ctx - 1, -(-(LONGEST_DOC - 1) // tok_rows))

    with jax.named_scope("kv_exchange"):
        own_docs = segments[0]
        doc_row = jnp.zeros((16, 2 * kv_width), jnp.bfloat16)
        doc_row = doc_row.at[0, :tok_rows].set(own_docs.astype(jnp.bfloat16))
        packed = jnp.concatenate(
            [jnp.concatenate([keys[0], values[0]], axis=1), doc_row], axis=0
        )
        core = lax.rem(ctx_index, 2)
        chip_back = -(-back // 2)
        fetched = {d: shifted(packed, "ctx", 2 * d, n_ctx) for d in range(chip_back, 0, -1)}
        split = chip_back // 2
        older = jnp.stack([fetched[d] for d in range(chip_back, split, -1)])
        newer = jnp.stack([fetched[d] for d in range(split, 0, -1)] + [packed])
        swap = [(i, i ^ 1) for i in range(n_ctx)]
        mine = [older, newer]
        assert sum(p.shape[0] for p in mine) == chip_back + 1
        theirs = [lax.ppermute(p, "ctx", swap) for p in mine]
        chip_of_block = jnp.concatenate([jnp.arange(-chip_back, 1, dtype=jnp.int32)] * 2)
        core_of_block = jnp.concatenate(
            [jnp.full((chip_back + 1,), 0, jnp.int32), jnp.full((chip_back + 1,), 1, jnp.int32)]
        )
        block_index = (ctx_index - core) + 2 * chip_of_block + lax.rem(core + core_of_block, 2)

    with jax.named_scope("attention"):
        key_pos = (
            block_index[:, None] * tok_rows + jnp.arange(tok_rows, dtype=jnp.int32)[None, :]
        ).reshape(-1)
        query_pos = first_pos + jnp.arange(tok_rows, dtype=jnp.int32)
        projected = attend(
            query_local, query_pos, own_docs, key_pos, mine + theirs, group_size, scale,
            out_weight[0],
        )

    with jax.named_scope("relay"):
        late_sent, projected = lax.optimization_barrier((sent, projected))
        arrived_stream = shifted(late_sent, "pipe", 1, n_pipe)[0]
        section_index = lax.axis_index("pipe")
        incoming = jnp.where(section_index == 0, late_sent[0], arrived_stream)

    with jax.named_scope("projection"):
        branch = ring_reduce_scatter(projected, n_tp)

    with jax.named_scope("norm"):
        square_sum = jnp.sum(branch * branch, axis=-1)
        mean_square = lax.psum(square_sum, "tp") / D
        normed = branch * lax.rsqrt(mean_square + 1e-06)[:, None] * norm_gain[0][None, :]
        emitted = (incoming.astype(jnp.float32) + normed).astype(jnp.bfloat16)
    return emitted[None]


def solution(mesh):
    return jax.shard_map(
        body,
        mesh=mesh,
        in_specs=(
            P("pipe", "ctx", "tp"),
            P("pipe", "ctx", "tp"),
            P("pipe", "ctx", "tp"),
            P("pipe", "ctx", "tp"),
            P("pipe", "ctx"),
            P("pipe", "tp", None),
            P("pipe", "tp"),
        ),
        out_specs=P("pipe", "ctx", "tp"),
        check_vma=False,
    )
```
